512 devices in a mesh: rep: 32 (over z_lo, x), seq: 16 (over z_hi, y, core).
Axes of the slice: x: 4, y: 4, z: 16 (z_hi: 2, z_lo: 8; z = z_hi * 8 + z_lo), core: 2. Of those that a mesh axis runs over, the one named last changes fastest.
Arguments:
- tokens: bfloat16 [32, 4096, 6144], P('rep', 'seq'), may hold values from -6 to 6
- queries: bfloat16 [32, 4096, 128], P('rep', 'seq'), may hold values from -4 to 4
- ctx_grad: bfloat16 [32, 4096, 128], P('rep', 'seq'), may hold values from -0.25 to 0.25
- kv_weight: bfloat16 [32, 6144, 256], P('rep', 'seq'), may hold values from -0.078125 to 0.078125
- rand_blocks: int32 [64, 3], replicated, may hold values from 0 to 63
- step_count: int32 [1], replicated, may hold values from 0 to 63
Outputs:
- mixed_update: float32 [32, 6144, 256], P('rep', 'seq')
- query_grad: bfloat16 [32, 4096, 128], P('rep', 'seq')
The draws below stay inside these ranges and needn't reach their ends.
Inputs may be any that keep to these rules, and one draw needn't show every extreme that they name: `rand_blocks`: block indices of the same replica sequence.
All inputs are finite; a program needn't handle non-finite values.
Results may differ from the reference program's by a relative error of at most 0.02.
Values may be sent and summed in bfloat16 or wider, within the bound.
No kernel may reach another device: no remote copies, remote signals or barrier semaphores. Data moves between devices by JAX's collectives and lax.ppermute only.
A program may use at most 64 MiB of HBM per device.

```python
import jax
import jax.numpy as jnp
from jax import lax

D = 6144
HD = 128
BLOCK = 64
RAND = 3
TOK_DEV = 256
TOKENS = 4096
NBLK = 64
N_REP = 32
N_SEQ = 16


def set_ends(result, stream_key, least, top_value):
    index_at = [jax.random.randint(jax.random.fold_in(stream_key, axis), (), 0, length) for axis, length in enumerate(result.shape)]
    longest = result.shape.index(max(result.shape))
    neighbour = index_at[:longest] + [(index_at[longest] + 1) % result.shape[longest]] + index_at[longest + 1:]
    return result.at[tuple(index_at)].set(least).at[tuple(neighbour)].set(top_value)


def block_scale(rng, dims, pieces, least, top_value):
    level, own = 1.0, jax.random.fold_in(rng, 6)
    for axis_at, shards_of in pieces:
        steps = jnp.exp(jax.random.uniform(jax.random.fold_in(own, axis_at), (shards_of,), jnp.float32, least / len(pieces), top_value / len(pieces)))
        level = level * jnp.repeat(steps, dims[axis_at] // shards_of).reshape([-1 if axis == axis_at else 1 for axis in range(len(dims))])
    return level


def bell_draw(stream_key, dims, deviation, bound, shards=(), kind=jnp.bfloat16):
    gain = block_scale(stream_key, dims, shards, -0.22, 0.18) if shards else 1.0
    entries = jax.random.normal(stream_key, dims, jnp.float32) * deviation * gain
    return jnp.minimum(jnp.maximum(entries, -bound), bound).astype(kind)


def setup_inputs(seed: int = 0) -> dict:
    splits = jax.random.split(jax.random.key(seed), 7)
    tokens = bell_draw(splits[0], (N_REP, TOKENS, D), 1.0, 6.0, ((0, 32), (1, 16)))
    queries = bell_draw(splits[1], (N_REP, TOKENS, HD), 0.5, 4.0, ((0, 32), (1, 16)))
    ctx_grad = bell_draw(splits[2], (N_REP, TOKENS, HD), (TOKENS ** -0.5), 0.25, ((0, 32), (1, 16)))
    kv_weight = bell_draw(splits[3], (N_REP, D, 2 * HD), D ** -0.5, 0.078125, ((0, 32), (1, 16)))
    rand_blocks = set_ends(jax.random.randint(splits[4], (NBLK, RAND), 0, NBLK), jax.random.fold_in(splits[4], 1), 0, NBLK - 1).astype(jnp.int32)
    step_count = jax.random.randint(splits[5], (1,), 0, 64).astype(jnp.int32)
    return {"tokens": tokens, "queries": queries, "ctx_grad": ctx_grad, "kv_weight": kv_weight, "rand_blocks": rand_blocks, "step_count": step_count}


def token_mask(rand_blocks):
    row_ids = jnp.arange(NBLK, dtype=jnp.int32)[:, None]
    col_ids = jnp.arange(NBLK, dtype=jnp.int32)[None, :]
    is_near = jnp.abs(row_ids - col_ids) <= 1
    picked = jnp.any(rand_blocks[:, :, None] == col_ids[:, None, :], axis=1)
    allowed = is_near | (col_ids == 0) | picked
    return jnp.repeat(jnp.repeat(allowed, BLOCK, axis=0), BLOCK, axis=1)


def one_replica(allowed, arrays):
    tok_rows, query_rows, grad_rows, weight_rows = arrays
    kv_rows = jnp.dot(tok_rows, weight_rows, preferred_element_type=jnp.float32).astype(jnp.bfloat16)
    keys_all = kv_rows[:, :HD]
    values_all = kv_rows[:, HD:]
    inv_root = HD ** -0.5
    scores = jnp.dot(query_rows, keys_all.T, preferred_element_type=jnp.float32) * inv_root
    unnorm = jnp.where(allowed, jnp.exp(scores), jnp.float32(0.0))
    row_total = jnp.sum(unnorm, axis=1, keepdims=True)
    prob_rows = unnorm / row_total
    prob_low = prob_rows.astype(jnp.bfloat16)
    context = jnp.dot(prob_low, values_all, preferred_element_type=jnp.float32)
    row_delta = jnp.sum(grad_rows.astype(jnp.float32) * context, axis=1, keepdims=True)
    prob_grad = jnp.dot(grad_rows, values_all.T, preferred_element_type=jnp.float32)
    score_grad = (prob_rows * (prob_grad - row_delta) * inv_root).astype(jnp.bfloat16)
    query_grad = jnp.dot(score_grad, keys_all, preferred_element_type=jnp.float32).astype(jnp.bfloat16)
    key_grad = jnp.dot(score_grad.T, query_rows, preferred_element_type=jnp.float32)
    value_grad = jnp.dot(prob_low.T, grad_rows, preferred_element_type=jnp.float32)
    kv_grad = jnp.concatenate([key_grad, value_grad], axis=1).astype(jnp.bfloat16)
    tok_split = tok_rows.reshape(N_SEQ, TOK_DEV, D)
    grad_split = kv_grad.reshape(N_SEQ, TOK_DEV, 2 * HD)

    def partial_sum(pair):
        return jnp.dot(pair[0].T, pair[1], preferred_element_type=jnp.float32).astype(jnp.bfloat16)

    partials = lax.map(partial_sum, (tok_split, grad_split))
    partials = lax.optimization_barrier(partials)
    weight_grad = jnp.sum(partials.astype(jnp.float32), axis=0)
    return weight_grad, query_grad


def reference(tokens, queries, ctx_grad, kv_weight, rand_blocks, step_count):
    allowed = token_mask(rand_blocks)
    weight_grad, query_grad = lax.map(lambda arrays: one_replica(allowed, arrays), (tokens, queries, ctx_grad, kv_weight))
    distance = jnp.left_shift(jnp.int32(1), step_count[0] % 4)
    mixed_update = (weight_grad + jnp.roll(weight_grad, distance, axis=0) + jnp.roll(weight_grad, -distance, axis=0)) / 3.0
    return mixed_update, query_grad
```

```python
from functools import partial

import jax
import jax.numpy as jnp
from jax import lax
from jax.sharding import Mesh
from jax.sharding import PartitionSpec as P

BLOCK = 64
SEQ_AXES = ("zh", "y", "c")


def for_sending(value):

    def short(part):
        return part.astype(jnp.bfloat16) if part.dtype == jnp.float32 else part

    return jax.tree.map(short, value)


def shifted(value, axis, steps):
    count = lax.axis_size(axis)
    pairs = [(source, (source + steps) % count) for source in range(count)]
    return lax.ppermute(value, axis, pairs)


def seq_position():
    return (lax.axis_index("zh") * lax.axis_size("y") + lax.axis_index("y")) * lax.axis_size(
        "c"
    ) + lax.axis_index("c")


def gather_seq(piece):
    step = lax.all_gather(piece, "zh", axis=0)
    step = lax.all_gather(step, "y", axis=0)
    step = lax.all_gather(step, "c", axis=0)
    step = jnp.transpose(step, (2, 1, 0) + tuple(range(3, step.ndim)))
    return step.reshape((-1,) + piece.shape[1:])


def scatter_seq(whole, first_type, later_type):
    zh_n, y_n, c_n = (lax.axis_size(name) for name in SEQ_AXES)
    rows = whole.shape[0] // (zh_n * y_n * c_n)
    parts = whole.reshape((zh_n, y_n, c_n, rows) + whole.shape[1:])
    parts = jnp.moveaxis(parts, 2, 0).astype(first_type)
    parts = lax.psum_scatter(parts, "c", scatter_dimension=0)
    parts = jnp.moveaxis(parts, 1, 0).astype(later_type)
    parts = lax.psum_scatter(parts, "y", scatter_dimension=0)
    mine = lax.axis_index("zh")
    other = 1 - mine
    keep = lax.dynamic_index_in_dim(parts, mine, 0, keepdims=False).astype(jnp.float32)
    send = lax.dynamic_index_in_dim(parts, other, 0, keepdims=False)
    got = lax.ppermute(send, "zh", [(0, 1), (1, 0)])
    return keep + got.astype(jnp.float32)


def fold_rows(tok_rows, row_piece):
    return jnp.dot(tok_rows, row_piece, preferred_element_type=jnp.float32)


def contract_rows(matrix_a, matrix_b):
    return lax.dot_general(
        matrix_a, matrix_b, (((0,), (0,)), ((), ())), preferred_element_type=jnp.float32
    )


def contract_cols(matrix_a, matrix_b):
    return lax.dot_general(
        matrix_a, matrix_b, (((1,), (1,)), ((), ())), preferred_element_type=jnp.float32
    )


def attend_mask(query_blocks, key_blocks, chosen_rows, blk_size):
    is_near = jnp.abs(query_blocks[:, None] - key_blocks[None, :]) <= 1
    picked = jnp.any(chosen_rows[:, :, None] == key_blocks[None, None, :], axis=1)
    allowed = is_near | (key_blocks[None, :] == 0) | picked
    return jnp.repeat(jnp.repeat(allowed, blk_size, axis=0), blk_size, axis=1)


def gossip(update, distance, rep_count):
    if distance == 0:
        return update
    from_low = jax.tree.map(
        lambda part, own: part.astype(own.dtype),
        shifted(for_sending(update), "rep", distance),
        update,
    )
    from_high = jax.tree.map(
        lambda part, own: part.astype(own.dtype),
        shifted(for_sending(update), "rep", rep_count - distance),
        update,
    )
    return (update + from_low + from_high) / 3.0


def per_device(tokens, queries, ctx_grad, kv_weight, rand_blocks, step_count):
    tokens_here = tokens[0]
    query_here = queries[0]
    grad_here = ctx_grad[0]
    weight_here = kv_weight[0]
    seq_count = lax.axis_size(SEQ_AXES)
    rep_count = lax.axis_size("rep")
    seq_index = seq_position()
    tok_count = tokens_here.shape[0]
    kv_width = weight_here.shape[1]
    head_size = kv_width // 2
    blk_size = BLOCK
    blocks_dev = tok_count // blk_size
    block_count = blocks_dev * seq_count
    inv_root = head_size ** (-0.5)
    kv_here = fold_rows(tokens_here, gather_seq(weight_here)).astype(jnp.bfloat16)
    kv_all = gather_seq(kv_here)
    keys_all = kv_all[:, :head_size]
    values_all = kv_all[:, head_size:]
    blocks_here = seq_index * blocks_dev + jnp.arange(blocks_dev, dtype=jnp.int32)
    every_block = jnp.arange(block_count, dtype=jnp.int32)
    chosen_here = lax.dynamic_slice_in_dim(rand_blocks, seq_index * blocks_dev, blocks_dev, 0)
    allowed = attend_mask(blocks_here, every_block, chosen_here, blk_size)
    scores = contract_cols(query_here, keys_all) * inv_root
    unnorm = jnp.where(allowed, jnp.exp(scores), jnp.float32(0.0))
    row_total = jnp.sum(unnorm, axis=1, keepdims=True)
    prob_rows = unnorm / row_total
    prob_low = prob_rows.astype(jnp.bfloat16)
    context = jnp.dot(prob_low, values_all, preferred_element_type=jnp.float32)
    row_delta = jnp.sum(grad_here.astype(jnp.float32) * context, axis=1, keepdims=True)
    prob_grad = contract_cols(grad_here, values_all)
    score_grad = (prob_rows * (prob_grad - row_delta) * inv_root).astype(jnp.bfloat16)
    query_grad = jnp.dot(score_grad, keys_all, preferred_element_type=jnp.float32).astype(
        jnp.bfloat16
    )
    key_terms = contract_rows(score_grad, query_here)
    value_terms = contract_rows(prob_low, grad_here)
    grad_terms = jnp.concatenate([key_terms, value_terms], axis=1)
    kv_grad = scatter_seq(grad_terms, jnp.float32, jnp.bfloat16).astype(jnp.bfloat16)
    grad_slice = scatter_seq(
        contract_rows(tokens_here, kv_grad).astype(jnp.bfloat16), jnp.float32, jnp.bfloat16
    )
    branches = [
        partial(gossip, distance=(1 << level_idx) % rep_count, rep_count=rep_count)
        for level_idx in range(4)
    ]
    mixed_update = lax.switch(step_count[0] % 4, branches, grad_slice)
    return (mixed_update[None], query_grad[None])


def solution(mesh):
    rep_n, seq_n = mesh.devices.shape
    sub_mesh = Mesh(mesh.devices.reshape(rep_n, 2, seq_n // 4, 2), ("rep",) + SEQ_AXES)
    return jax.shard_map(
        per_device,
        mesh=sub_mesh,
        in_specs=(
            P("rep", SEQ_AXES, None),
            P("rep", SEQ_AXES, None),
            P("rep", SEQ_AXES, None),
            P("rep", SEQ_AXES, None),
            P(),
            P(),
        ),
        out_specs=(P("rep", SEQ_AXES, None), P("rep", SEQ_AXES, None)),
        check_vma=False,
    )
```

```python
from functools import partial

import jax
import jax.numpy as jnp
from jax import lax
from jax.sharding import Mesh
from jax.sharding import PartitionSpec as P

BLOCK = 64
SEQ_AXES = ("zh", "y", "c")


def for_sending(value):

    def short(part):
        return part.astype(jnp.bfloat16) if part.dtype == jnp.float32 else part

    return jax.tree.map(short, value)


def shifted(value, axis, steps):
    count = lax.axis_size(axis)
    pairs = [(source, (source + steps) % count) for source in range(count)]
    return lax.ppermute(value, axis, pairs)


def seq_position():
    return (lax.axis_index("zh") * lax.axis_size("y") + lax.axis_index("y")) * lax.axis_size(
        "c"
    ) + lax.axis_index("c")


def swap_zh(value):
    return lax.ppermute(value, "zh", [(0, 1), (1, 0)])


def spread_half(piece):
    count = lax.axis_size("y") * lax.axis_size("c")
    copies = jnp.broadcast_to(piece[None], (count,) + piece.shape)
    return lax.all_to_all(copies, ("y", "c"), 0, 0, tiled=False)


def gather_seq(piece):
    from_other = swap_zh(piece)
    own_half = spread_half(piece)
    other_half = spread_half(from_other)
    first_own = lax.axis_index("zh") == 0
    low = jnp.where(first_own, own_half, other_half)
    high = jnp.where(first_own, other_half, own_half)
    return jnp.concatenate([low, high]).reshape((-1,) + piece.shape[1:])


def reduce_half(part):
    core = lax.axis_index("c")
    keep = lax.dynamic_index_in_dim(part, core, 1, keepdims=False)
    send = lax.dynamic_index_in_dim(part, 1 - core, 1, keepdims=False)
    got = lax.ppermute(send, "c", [(0, 1), (1, 0)])
    summed = (keep.astype(jnp.float32) + got.astype(jnp.float32)).astype(jnp.bfloat16)
    spread = lax.all_to_all(summed, "y", 0, 0, tiled=False)
    return jnp.sum(spread.astype(jnp.float32), axis=0)


def scatter_seq(whole):
    zh_n, y_n, c_n = (lax.axis_size(name) for name in SEQ_AXES)
    rows = whole.shape[0] // (zh_n * y_n * c_n)
    parts = whole.reshape((zh_n, y_n, c_n, rows) + whole.shape[1:])
    mine = lax.axis_index("zh")
    for_other = reduce_half(lax.dynamic_index_in_dim(parts, 1 - mine, 0, keepdims=False))
    got = swap_zh(for_other.astype(jnp.bfloat16))
    for_me = reduce_half(lax.dynamic_index_in_dim(parts, mine, 0, keepdims=False))
    return for_me + got.astype(jnp.float32)


def fold_rows(tok_rows, row_piece):
    return jnp.dot(tok_rows, row_piece, preferred_element_type=jnp.float32)


def contract_rows(matrix_a, matrix_b):
    return lax.dot_general(
        matrix_a, matrix_b, (((0,), (0,)), ((), ())), preferred_element_type=jnp.float32
    )


def contract_cols(matrix_a, matrix_b):
    return lax.dot_general(
        matrix_a, matrix_b, (((1,), (1,)), ((), ())), preferred_element_type=jnp.float32
    )


def attend_mask(query_blocks, key_blocks, chosen_rows, blk_size):
    is_near = jnp.abs(query_blocks[:, None] - key_blocks[None, :]) <= 1
    picked = jnp.any(chosen_rows[:, :, None] == key_blocks[None, None, :], axis=1)
    allowed = is_near | (key_blocks[None, :] == 0) | picked
    return jnp.repeat(jnp.repeat(allowed, blk_size, axis=0), blk_size, axis=1)


def gossip(update, distance, rep_count):
    if distance == 0:
        return update
    from_low = jax.tree.map(
        lambda part, own: part.astype(own.dtype),
        shifted(for_sending(update), "rep", distance),
        update,
    )
    from_high = jax.tree.map(
        lambda part, own: part.astype(own.dtype),
        shifted(for_sending(update), "rep", rep_count - distance),
        update,
    )
    return (update + from_low + from_high) / 3.0


def per_device(tokens, queries, ctx_grad, kv_weight, rand_blocks, step_count):
    tokens_here = tokens[0]
    query_here = queries[0]
    grad_here = ctx_grad[0]
    weight_here = kv_weight[0]
    seq_count = lax.axis_size(SEQ_AXES)
    rep_count = lax.axis_size("rep")
    seq_index = seq_position()
    tok_count = tokens_here.shape[0]
    kv_width = weight_here.shape[1]
    head_size = kv_width // 2
    blk_size = BLOCK
    blocks_dev = tok_count // blk_size
    block_count = blocks_dev * seq_count
    inv_root = head_size ** (-0.5)
    kv_here = fold_rows(tokens_here, gather_seq(weight_here)).astype(jnp.bfloat16)
    kv_all = gather_seq(kv_here)
    keys_all = kv_all[:, :head_size]
    values_all = kv_all[:, head_size:]
    blocks_here = seq_index * blocks_dev + jnp.arange(blocks_dev, dtype=jnp.int32)
    every_block = jnp.arange(block_count, dtype=jnp.int32)
    chosen_here = lax.dynamic_slice_in_dim(rand_blocks, seq_index * blocks_dev, blocks_dev, 0)
    allowed = attend_mask(blocks_here, every_block, chosen_here, blk_size)
    scores = contract_cols(query_here, keys_all) * inv_root
    unnorm = jnp.where(allowed, jnp.exp(scores), jnp.float32(0.0))
    row_total = jnp.sum(unnorm, axis=1, keepdims=True)
    prob_rows = unnorm / row_total
    prob_low = prob_rows.astype(jnp.bfloat16)
    context = jnp.dot(prob_low, values_all, preferred_element_type=jnp.float32)
    row_delta = jnp.sum(grad_here.astype(jnp.float32) * context, axis=1, keepdims=True)
    prob_grad = contract_cols(grad_here, values_all)
    score_grad = (prob_rows * (prob_grad - row_delta) * inv_root).astype(jnp.bfloat16)
    query_grad = jnp.dot(score_grad, keys_all, preferred_element_type=jnp.float32).astype(
        jnp.bfloat16
    )
    key_terms = contract_rows(score_grad, query_here)
    value_terms = contract_rows(prob_low, grad_here)
    grad_terms = jnp.concatenate([key_terms, value_terms], axis=1)
    kv_grad = scatter_seq(grad_terms.astype(jnp.bfloat16)).astype(jnp.bfloat16)
    grad_slice = scatter_seq(contract_rows(tokens_here, kv_grad).astype(jnp.bfloat16))
    branches = [
        partial(gossip, distance=(1 << level_idx) % rep_count, rep_count=rep_count)
        for level_idx in range(4)
    ]
    mixed_update = lax.switch(step_count[0] % 4, branches, grad_slice)
    return (mixed_update[None], query_grad[None])


def solution(mesh):
    rep_n, seq_n = mesh.devices.shape
    sub_mesh = Mesh(mesh.devices.reshape(rep_n, 2, seq_n // 4, 2), ("rep",) + SEQ_AXES)
    return jax.shard_map(
        per_device,
        mesh=sub_mesh,
        in_specs=(
            P("rep", SEQ_AXES, None),
            P("rep", SEQ_AXES, None),
            P("rep", SEQ_AXES, None),
            P("rep", SEQ_AXES, None),
            P(),
            P(),
        ),
        out_specs=(P("rep", SEQ_AXES, None), P("rep", SEQ_AXES, None)),
        check_vma=False,
    )
```

```python
from functools import partial

import jax
import jax.numpy as jnp
from jax import lax
from jax.sharding import Mesh
from jax.sharding import PartitionSpec as P

BLOCK = 64
SEQ_AXES = ("zh", "y", "c")


def for_sending(value):

    def short(part):
        return part.astype(jnp.bfloat16) if part.dtype == jnp.float32 else part

    return jax.tree.map(short, value)


def shifted(value, axis, steps):
    count = lax.axis_size(axis)
    pairs = [(source, (source + steps) % count) for source in range(count)]
    return lax.ppermute(value, axis, pairs)


def seq_position():
    return (lax.axis_index("zh") * lax.axis_size("y") + lax.axis_index("y")) * lax.axis_size(
        "c"
    ) + lax.axis_index("c")


def swap_zh(value):
    return lax.ppermute(value, "zh", [(0, 1), (1, 0)])


def spread_half(piece):
    count = lax.axis_size("y") * lax.axis_size("c")
    copies = jnp.broadcast_to(piece[None], (count,) + piece.shape)
    return lax.all_to_all(copies, ("y", "c"), 0, 0, tiled=False)


def gather_seq(piece):
    from_other = swap_zh(piece)
    own_half = spread_half(piece)
    other_half = spread_half(from_other)
    first_own = lax.axis_index("zh") == 0
    low = jnp.where(first_own, own_half, other_half)
    high = jnp.where(first_own, other_half, own_half)
    return jnp.concatenate([low, high]).reshape((-1,) + piece.shape[1:])


def gather_other_first(piece):
    from_other = swap_zh(piece)
    own_half = spread_half(piece)
    other_half = spread_half(from_other)
    return jnp.concatenate([other_half, own_half]).reshape((-1,) + piece.shape[1:])


def reduce_half(part):
    paired = lax.all_to_all(part, "c", 1, 1, tiled=False)
    summed = jnp.sum(paired.astype(jnp.float32), axis=1).astype(jnp.bfloat16)
    spread = lax.all_to_all(summed, "y", 0, 0, tiled=False)
    return jnp.sum(spread.astype(jnp.float32), axis=0)


def scatter_halves(for_other, for_me):
    y_n, c_n = lax.axis_size("y"), lax.axis_size("c")
    shape = (y_n, c_n, for_other.shape[0] // (y_n * c_n)) + for_other.shape[1:]
    got = swap_zh(reduce_half(for_other.reshape(shape)).astype(jnp.bfloat16))
    return reduce_half(for_me.reshape(shape)) + got.astype(jnp.float32)


def fold_rows(tok_rows, row_piece):
    return jnp.dot(tok_rows, row_piece, preferred_element_type=jnp.float32)


def contract_rows(matrix_a, matrix_b):
    return lax.dot_general(
        matrix_a, matrix_b, (((0,), (0,)), ((), ())), preferred_element_type=jnp.float32
    )


def contract_cols(matrix_a, matrix_b):
    return lax.dot_general(
        matrix_a, matrix_b, (((1,), (1,)), ((), ())), preferred_element_type=jnp.float32
    )


def attend_mask(query_blocks, key_blocks, chosen_rows, blk_size):
    is_near = jnp.abs(query_blocks[:, None] - key_blocks[None, :]) <= 1
    picked = jnp.any(chosen_rows[:, :, None] == key_blocks[None, None, :], axis=1)
    allowed = is_near | (key_blocks[None, :] == 0) | picked
    return jnp.repeat(jnp.repeat(allowed, blk_size, axis=0), blk_size, axis=1)


def gossip(update, distance, rep_count):
    if distance == 0:
        return update
    from_low = jax.tree.map(
        lambda part, own: part.astype(own.dtype),
        shifted(for_sending(update), "rep", distance),
        update,
    )
    from_high = jax.tree.map(
        lambda part, own: part.astype(own.dtype),
        shifted(for_sending(update), "rep", rep_count - distance),
        update,
    )
    return (update + from_low + from_high) / 3.0


def per_device(tokens, queries, ctx_grad, kv_weight, rand_blocks, step_count):
    tokens_here = tokens[0]
    query_here = queries[0]
    grad_here = ctx_grad[0]
    weight_here = kv_weight[0]
    seq_count = lax.axis_size(SEQ_AXES)
    rep_count = lax.axis_size("rep")
    seq_index = seq_position()
    tok_count = tokens_here.shape[0]
    kv_width = weight_here.shape[1]
    head_size = kv_width // 2
    blk_size = BLOCK
    blocks_dev = tok_count // blk_size
    inv_root = head_size ** (-0.5)
    kv_here = fold_rows(tokens_here, gather_seq(weight_here)).astype(jnp.bfloat16)
    kv_all = gather_other_first(kv_here)
    keys_all = kv_all[:, :head_size]
    values_all = kv_all[:, head_size:]
    half_n = seq_count // 2
    my_half = lax.axis_index("zh")
    order = jnp.concatenate([(1 - my_half) * half_n + jnp.arange(half_n), my_half * half_n + jnp.arange(half_n)])
    every_block = (order[:, None] * blocks_dev + jnp.arange(blocks_dev)[None, :]).reshape(-1).astype(jnp.int32)
    blocks_here = seq_index * blocks_dev + jnp.arange(blocks_dev, dtype=jnp.int32)
    chosen_here = lax.dynamic_slice_in_dim(rand_blocks, seq_index * blocks_dev, blocks_dev, 0)
    allowed = attend_mask(blocks_here, every_block, chosen_here, blk_size)
    scores = contract_cols(query_here, keys_all) * inv_root
    unnorm = jnp.where(allowed, jnp.exp(scores), jnp.float32(0.0))
    row_total = jnp.sum(unnorm, axis=1, keepdims=True)
    prob_rows = unnorm / row_total
    prob_low = prob_rows.astype(jnp.bfloat16)
    context = jnp.dot(prob_low, values_all, preferred_element_type=jnp.float32)
    row_delta = jnp.sum(grad_here.astype(jnp.float32) * context, axis=1, keepdims=True)
    prob_grad = contract_cols(grad_here, values_all)
    score_grad = (prob_rows * (prob_grad - row_delta) * inv_root).astype(jnp.bfloat16)
    query_grad = jnp.dot(score_grad, keys_all, preferred_element_type=jnp.float32).astype(
        jnp.bfloat16
    )
    key_terms = contract_rows(score_grad, query_here)
    value_terms = contract_rows(prob_low, grad_here)
    grad_terms = jnp.concatenate([key_terms, value_terms], axis=1).astype(jnp.bfloat16)
    half_rows = grad_terms.shape[0] // 2
    kv_grad = scatter_halves(grad_terms[:half_rows], grad_terms[half_rows:]).astype(jnp.bfloat16)
    tok_view = tokens_here.reshape(tok_count, 2, -1)
    tok_other = lax.dynamic_index_in_dim(tok_view, 1 - my_half, 1, keepdims=False)
    tok_mine = lax.dynamic_index_in_dim(tok_view, my_half, 1, keepdims=False)
    grad_slice = scatter_halves(
        contract_rows(tok_other, kv_grad).astype(jnp.bfloat16),
        contract_rows(tok_mine, kv_grad).astype(jnp.bfloat16),
    )
    branches = [
        partial(gossip, distance=(1 << level_idx) % rep_count, rep_count=rep_count)
        for level_idx in range(4)
    ]
    mixed_update = lax.switch(step_count[0] % 4, branches, grad_slice)
    return (mixed_update[None], query_grad[None])


def solution(mesh):
    rep_n, seq_n = mesh.devices.shape
    sub_mesh = Mesh(mesh.devices.reshape(rep_n, 2, seq_n // 4, 2), ("rep",) + SEQ_AXES)
    return jax.shard_map(
        per_device,
        mesh=sub_mesh,
        in_specs=(
            P("rep", SEQ_AXES, None),
            P("rep", SEQ_AXES, None),
            P("rep", SEQ_AXES, None),
            P("rep", SEQ_AXES, None),
            P(),
            P(),
        ),
        out_specs=(P("rep", SEQ_AXES, None), P("rep", SEQ_AXES, None)),
        check_vma=False,
    )
```

```python
from functools import partial

import jax
import jax.numpy as jnp
from jax import lax
from jax.sharding import Mesh
from jax.sharding import PartitionSpec as P

BLOCK = 64
SEQ_AXES = ("zh", "y", "c")


def for_sending(value):

    def short(part):
        return part.astype(jnp.bfloat16) if part.dtype == jnp.float32 else part

    return jax.tree.map(short, value)


def shifted(value, axis, steps):
    count = lax.axis_size(axis)
    pairs = [(source, (source + steps) % count) for source in range(count)]
    return lax.ppermute(value, axis, pairs)


def seq_position():
    return (lax.axis_index("zh") * lax.axis_size("y") + lax.axis_index("y")) * lax.axis_size(
        "c"
    ) + lax.axis_index("c")


def swap_zh(value):
    return lax.ppermute(value, "zh", [(0, 1), (1, 0)])


def spread_half(piece):
    count = lax.axis_size("y") * lax.axis_size("c")
    copies = jnp.broadcast_to(piece[None], (count,) + piece.shape)
    return lax.all_to_all(copies, ("y", "c"), 0, 0, tiled=False)


def gather_seq(piece):
    from_other = swap_zh(piece)
    own_half = spread_half(piece)
    other_half = spread_half(from_other)
    first_own = lax.axis_index("zh") == 0
    low = jnp.where(first_own, own_half, other_half)
    high = jnp.where(first_own, other_half, own_half)
    return jnp.concatenate([low, high]).reshape((-1,) + piece.shape[1:])


def gather_other_first(piece):
    from_other = swap_zh(piece)
    own_half = spread_half(piece)
    other_half = spread_half(from_other)
    return jnp.concatenate([other_half, own_half]).reshape((-1,) + piece.shape[1:])


def reduce_half(part):
    paired = lax.all_to_all(part, "c", 1, 1, tiled=False)
    summed = jnp.sum(paired.astype(jnp.float32), axis=1).astype(jnp.bfloat16)
    spread = lax.all_to_all(summed, "y", 0, 0, tiled=False)
    return jnp.sum(spread.astype(jnp.float32), axis=0)


def scatter_halves(for_other, for_me):
    y_n, c_n = lax.axis_size("y"), lax.axis_size("c")
    shape = (y_n, c_n, for_other.shape[0] // (y_n * c_n)) + for_other.shape[1:]
    got = swap_zh(reduce_half(for_other.reshape(shape)).astype(jnp.bfloat16))
    return reduce_half(for_me.reshape(shape)) + got.astype(jnp.float32)


def fold_rows(tok_rows, row_piece):
    return jnp.dot(tok_rows, row_piece, preferred_element_type=jnp.float32)


def contract_rows(matrix_a, matrix_b):
    return lax.dot_general(
        matrix_a, matrix_b, (((0,), (0,)), ((), ())), preferred_element_type=jnp.float32
    )


def contract_cols(matrix_a, matrix_b):
    return lax.dot_general(
        matrix_a, matrix_b, (((1,), (1,)), ((), ())), preferred_element_type=jnp.float32
    )


def attend_mask(query_blocks, key_blocks, chosen_rows, blk_size):
    is_near = jnp.abs(query_blocks[:, None] - key_blocks[None, :]) <= 1
    picked = jnp.any(chosen_rows[:, :, None] == key_blocks[None, None, :], axis=1)
    allowed = is_near | (key_blocks[None, :] == 0) | picked
    return jnp.repeat(jnp.repeat(allowed, blk_size, axis=0), blk_size, axis=1)


def gossip(update, distance, rep_count):
    if distance == 0:
        return update
    from_low = jax.tree.map(
        lambda part, own: part.astype(own.dtype),
        shifted(for_sending(update), "rep", distance),
        update,
    )
    from_high = jax.tree.map(
        lambda part, own: part.astype(own.dtype),
        shifted(for_sending(update), "rep", rep_count - distance),
        update,
    )
    return (update + from_low + from_high) / 3.0


def per_device(tokens, queries, ctx_grad, kv_weight, rand_blocks, step_count):
    tokens_here = tokens[0]
    query_here = queries[0]
    grad_here = ctx_grad[0]
    weight_here = kv_weight[0]
    seq_count = lax.axis_size(SEQ_AXES)
    rep_count = lax.axis_size("rep")
    seq_index = seq_position()
    tok_count = tokens_here.shape[0]
    kv_width = weight_here.shape[1]
    head_size = kv_width // 2
    blk_size = BLOCK
    blocks_dev = tok_count // blk_size
    inv_root = head_size ** (-0.5)
    keys_here = fold_rows(tokens_here, gather_seq(weight_here[:, :head_size])).astype(jnp.bfloat16)
    values_here = fold_rows(tokens_here, gather_seq(weight_here[:, head_size:])).astype(
        jnp.bfloat16
    )
    keys_all = gather_other_first(keys_here)
    values_all = gather_other_first(values_here)
    half_n = seq_count // 2
    my_half = lax.axis_index("zh")
    order = jnp.concatenate([(1 - my_half) * half_n + jnp.arange(half_n), my_half * half_n + jnp.arange(half_n)])
    every_block = (order[:, None] * blocks_dev + jnp.arange(blocks_dev)[None, :]).reshape(-1).astype(jnp.int32)
    blocks_here = seq_index * blocks_dev + jnp.arange(blocks_dev, dtype=jnp.int32)
    chosen_here = lax.dynamic_slice_in_dim(rand_blocks, seq_index * blocks_dev, blocks_dev, 0)
    allowed = attend_mask(blocks_here, every_block, chosen_here, blk_size)
    scores = contract_cols(query_here, keys_all) * inv_root
    unnorm = jnp.where(allowed, jnp.exp(scores), jnp.float32(0.0))
    row_total = jnp.sum(unnorm, axis=1, keepdims=True)
    prob_rows = unnorm / row_total
    prob_low = prob_rows.astype(jnp.bfloat16)
    context = jnp.dot(prob_low, values_all, preferred_element_type=jnp.float32)
    row_delta = jnp.sum(grad_here.astype(jnp.float32) * context, axis=1, keepdims=True)
    prob_grad = contract_cols(grad_here, values_all)
    score_grad = (prob_rows * (prob_grad - row_delta) * inv_root).astype(jnp.bfloat16)
    query_grad = jnp.dot(score_grad, keys_all, preferred_element_type=jnp.float32).astype(
        jnp.bfloat16
    )
    value_terms = contract_rows(prob_low, grad_here).astype(jnp.bfloat16)
    key_terms = contract_rows(score_grad, query_here).astype(jnp.bfloat16)
    half_rows = key_terms.shape[0] // 2
    value_grad = scatter_halves(value_terms[:half_rows], value_terms[half_rows:])
    key_grad = scatter_halves(key_terms[:half_rows], key_terms[half_rows:])
    tok_view = tokens_here.reshape(tok_count, 2, -1)
    tok_other = lax.dynamic_index_in_dim(tok_view, 1 - my_half, 1, keepdims=False)
    tok_mine = lax.dynamic_index_in_dim(tok_view, my_half, 1, keepdims=False)

    def weight_part(column_grad):
        column_grad = column_grad.astype(jnp.bfloat16)
        return scatter_halves(
            contract_rows(tok_other, column_grad).astype(jnp.bfloat16),
            contract_rows(tok_mine, column_grad).astype(jnp.bfloat16),
        )

    grad_slice = jnp.concatenate([weight_part(key_grad), weight_part(value_grad)], axis=1)
    branches = [
        partial(gossip, distance=(1 << level_idx) % rep_count, rep_count=rep_count)
        for level_idx in range(4)
    ]
    mixed_update = lax.switch(step_count[0] % 4, branches, grad_slice)
    return (mixed_update[None], query_grad[None])


def solution(mesh):
    rep_n, seq_n = mesh.devices.shape
    sub_mesh = Mesh(mesh.devices.reshape(rep_n, 2, seq_n // 4, 2), ("rep",) + SEQ_AXES)
    return jax.shard_map(
        per_device,
        mesh=sub_mesh,
        in_specs=(
            P("rep", SEQ_AXES, None),
            P("rep", SEQ_AXES, None),
            P("rep", SEQ_AXES, None),
            P("rep", SEQ_AXES, None),
            P(),
            P(),
        ),
        out_specs=(P("rep", SEQ_AXES, None), P("rep", SEQ_AXES, None)),
        check_vma=False,
    )
```

```python
from functools import partial

import jax
import jax.numpy as jnp
from jax import lax
from jax.sharding import Mesh
from jax.sharding import PartitionSpec as P


BLOCK = 64
SEQ_AXES = ("zh", "y", "c")


def for_sending(value):

    def short(part):
        return part.astype(jnp.bfloat16) if part.dtype == jnp.float32 else part

    return jax.tree.map(short, value)


def shifted(value, axis, steps):
    count = lax.axis_size(axis)
    pairs = [(source, (source + steps) % count) for source in range(count)]
    return lax.ppermute(value, axis, pairs)


def seq_position():
    return (lax.axis_index("zh") * lax.axis_size("y") + lax.axis_index("y")) * lax.axis_size(
        "c"
    ) + lax.axis_index("c")


def swap_zh(value):
    return lax.ppermute(value, "zh", [(0, 1), (1, 0)])


def spread_half(piece):
    count = lax.axis_size("y") * lax.axis_size("c")
    copies = jnp.broadcast_to(piece[None], (count,) + piece.shape)
    return lax.all_to_all(copies, ("y", "c"), 0, 0, tiled=False)


def gather_seq(piece):
    from_other = swap_zh(piece)
    own_half = spread_half(piece)
    other_half = spread_half(from_other)
    first_own = lax.axis_index("zh") == 0
    low = jnp.where(first_own, own_half, other_half)
    high = jnp.where(first_own, other_half, own_half)
    return jnp.concatenate([low, high]).reshape((-1,) + piece.shape[1:])


def gather_other_first(piece):
    from_other = swap_zh(piece)
    own_half = spread_half(piece)
    other_half = spread_half(from_other)
    return jnp.concatenate([other_half, own_half]).reshape((-1,) + piece.shape[1:])


def reduce_half(part):
    paired = lax.all_to_all(part, "c", 1, 1, tiled=False)
    summed = jnp.sum(paired.astype(jnp.float32), axis=1).astype(jnp.bfloat16)
    spread = lax.all_to_all(summed, "y", 0, 0, tiled=False)
    return jnp.sum(spread.astype(jnp.float32), axis=0)


def scatter_halves(for_other, for_me):
    y_n, c_n = lax.axis_size("y"), lax.axis_size("c")
    shape = (y_n, c_n, for_other.shape[0] // (y_n * c_n)) + for_other.shape[1:]
    reduced = reduce_half(for_other.reshape(shape)).astype(jnp.bfloat16)
    got = swap_zh(reduced)
    kept = reduce_half(for_me.reshape(shape))
    return kept + got.astype(jnp.float32)


def fold_rows(tok_rows, row_piece):
    return jnp.dot(tok_rows, row_piece, preferred_element_type=jnp.float32)


def contract_rows(matrix_a, matrix_b):
    return lax.dot_general(
        matrix_a, matrix_b, (((0,), (0,)), ((), ())), preferred_element_type=jnp.float32
    )


def contract_cols(matrix_a, matrix_b):
    return lax.dot_general(
        matrix_a, matrix_b, (((1,), (1,)), ((), ())), preferred_element_type=jnp.float32
    )


def attend_mask(query_blocks, key_blocks, chosen_rows, blk_size):
    is_near = jnp.abs(query_blocks[:, None] - key_blocks[None, :]) <= 1
    picked = jnp.any(chosen_rows[:, :, None] == key_blocks[None, None, :], axis=1)
    allowed = is_near | (key_blocks[None, :] == 0) | picked
    return jnp.repeat(jnp.repeat(allowed, blk_size, axis=0), blk_size, axis=1)


def gossip(update, distance, rep_count):
    if distance == 0:
        return update
    from_low = jax.tree.map(
        lambda part, own: part.astype(own.dtype),
        shifted(for_sending(update), "rep", distance),
        update,
    )
    from_high = jax.tree.map(
        lambda part, own: part.astype(own.dtype),
        shifted(for_sending(update), "rep", rep_count - distance),
        update,
    )
    return (update + from_low + from_high) / 3.0


def per_device(tokens, queries, ctx_grad, kv_weight, rand_blocks, step_count):
    tokens_here = tokens[0]
    query_here = queries[0]
    grad_here = ctx_grad[0]
    weight_here = kv_weight[0]
    seq_count = lax.axis_size(SEQ_AXES)
    rep_count = lax.axis_size("rep")
    seq_index = seq_position()
    tok_count = tokens_here.shape[0]
    kv_width = weight_here.shape[1]
    head_size = kv_width // 2
    blk_size = BLOCK
    blocks_dev = tok_count // blk_size
    inv_root = head_size ** (-0.5)
    kv_here = fold_rows(tokens_here, gather_seq(weight_here)).astype(jnp.bfloat16)
    kv_all = gather_other_first(kv_here)
    keys_all = kv_all[:, :head_size]
    values_all = kv_all[:, head_size:]
    half_n = seq_count // 2
    my_half = lax.axis_index("zh")
    order = jnp.concatenate([(1 - my_half) * half_n + jnp.arange(half_n), my_half * half_n + jnp.arange(half_n)])
    every_block = (order[:, None] * blocks_dev + jnp.arange(blocks_dev)[None, :]).reshape(-1).astype(jnp.int32)
    blocks_here = seq_index * blocks_dev + jnp.arange(blocks_dev, dtype=jnp.int32)
    chosen_here = lax.dynamic_slice_in_dim(rand_blocks, seq_index * blocks_dev, blocks_dev, 0)
    allowed = attend_mask(blocks_here, every_block, chosen_here, blk_size)
    scores = contract_cols(query_here, keys_all) * inv_root
    unnorm = jnp.where(allowed, jnp.exp(scores), jnp.float32(0.0))
    row_total = jnp.sum(unnorm, axis=1, keepdims=True)
    prob_rows = unnorm / row_total
    prob_low = prob_rows.astype(jnp.bfloat16)
    context = jnp.dot(prob_low, values_all, preferred_element_type=jnp.float32)
    row_delta = jnp.sum(grad_here.astype(jnp.float32) * context, axis=1, keepdims=True)
    prob_grad = contract_cols(grad_here, values_all)
    score_grad = (prob_rows * (prob_grad - row_delta) * inv_root).astype(jnp.bfloat16)
    query_grad = jnp.dot(score_grad, keys_all, preferred_element_type=jnp.float32).astype(
        jnp.bfloat16
    )
    key_terms = contract_rows(score_grad, query_here)
    value_terms = contract_rows(prob_low, grad_here)
    grad_terms = jnp.concatenate([key_terms, value_terms], axis=1).astype(jnp.bfloat16)
    half_rows = grad_terms.shape[0] // 2
    kv_grad = scatter_halves(grad_terms[:half_rows], grad_terms[half_rows:]).astype(jnp.bfloat16)
    tok_view = tokens_here.reshape(tok_count, 2, -1)
    tok_other = lax.dynamic_index_in_dim(tok_view, 1 - my_half, 1, keepdims=False)
    tok_mine = lax.dynamic_index_in_dim(tok_view, my_half, 1, keepdims=False)
    grad_slice = scatter_halves(
        contract_rows(tok_other, kv_grad).astype(jnp.bfloat16),
        contract_rows(tok_mine, kv_grad).astype(jnp.bfloat16),
    )
    branches = [
        partial(gossip, distance=(1 << level_idx) % rep_count, rep_count=rep_count)
        for level_idx in range(4)
    ]
    mixed_update = lax.switch(step_count[0] % 4, branches, grad_slice)
    return (mixed_update[None], query_grad[None])


def solution(mesh):
    rep_n, seq_n = mesh.devices.shape
    sub_mesh = Mesh(mesh.devices.reshape(rep_n, 2, seq_n // 4, 2), ("rep",) + SEQ_AXES)
    return jax.shard_map(
        per_device,
        mesh=sub_mesh,
        in_specs=(
            P("rep", SEQ_AXES, None),
            P("rep", SEQ_AXES, None),
            P("rep", SEQ_AXES, None),
            P("rep", SEQ_AXES, None),
            P(),
            P(),
        ),
        out_specs=(P("rep", SEQ_AXES, None), P("rep", SEQ_AXES, None)),
        check_vma=False,
    )
```

```python
from functools import partial

import jax
import jax.numpy as jnp
from jax import lax
from jax.sharding import Mesh
from jax.sharding import PartitionSpec as P


BLOCK = 64
SEQ_AXES = ("zh", "y", "c")


def for_sending(value):

    def short(part):
        return part.astype(jnp.bfloat16) if part.dtype == jnp.float32 else part

    return jax.tree.map(short, value)


def shifted(value, axis, steps):
    count = lax.axis_size(axis)
    pairs = [(source, (source + steps) % count) for source in range(count)]
    return lax.ppermute(value, axis, pairs)


def seq_position():
    return (lax.axis_index("zh") * lax.axis_size("y") + lax.axis_index("y")) * lax.axis_size(
        "c"
    ) + lax.axis_index("c")


def swap_zh(value):
    return lax.ppermute(value, "zh", [(0, 1), (1, 0)])


def spread_half(piece):
    count = lax.axis_size("y") * lax.axis_size("c")
    copies = jnp.broadcast_to(piece[None], (count,) + piece.shape)
    return lax.all_to_all(copies, ("y", "c"), 0, 0, tiled=False)


def gather_seq(piece):
    from_other = swap_zh(piece)
    own_half = spread_half(piece)
    other_half = spread_half(from_other)
    first_own = lax.axis_index("zh") == 0
    low = jnp.where(first_own, own_half, other_half)
    high = jnp.where(first_own, other_half, own_half)
    return jnp.concatenate([low, high]).reshape((-1,) + piece.shape[1:])


def gather_other_first(piece):
    from_other = swap_zh(piece)
    own_half = spread_half(piece)
    other_half = spread_half(from_other)
    return jnp.concatenate([other_half, own_half]).reshape((-1,) + piece.shape[1:])


def reduce_half(part):
    first_core = lax.axis_index("c") == 0
    keep = jnp.where(first_core, part[:, 0], part[:, 1])
    send = jnp.where(first_core, part[:, 1], part[:, 0])
    got = lax.ppermute(send, "c", [(0, 1), (1, 0)])
    summed = (keep.astype(jnp.float32) + got.astype(jnp.float32)).astype(jnp.bfloat16)
    spread = lax.all_to_all(summed, "y", 0, 0, tiled=False)
    return jnp.sum(spread.astype(jnp.float32), axis=0)


def scatter_halves(for_other, for_me):
    y_n, c_n = lax.axis_size("y"), lax.axis_size("c")
    shape = (y_n, c_n, for_other.shape[0] // (y_n * c_n)) + for_other.shape[1:]
    reduced = reduce_half(for_other.reshape(shape)).astype(jnp.bfloat16)
    got = swap_zh(reduced)
    kept = reduce_half(for_me.reshape(shape))
    return kept + got.astype(jnp.float32)


def fold_rows(tok_rows, row_piece):
    return jnp.dot(tok_rows, row_piece, preferred_element_type=jnp.float32)


def contract_rows(matrix_a, matrix_b):
    return lax.dot_general(
        matrix_a, matrix_b, (((0,), (0,)), ((), ())), preferred_element_type=jnp.float32
    )


def contract_cols(matrix_a, matrix_b):
    return lax.dot_general(
        matrix_a, matrix_b, (((1,), (1,)), ((), ())), preferred_element_type=jnp.float32
    )


def attend_mask(query_blocks, key_blocks, chosen_rows, blk_size):
    is_near = jnp.abs(query_blocks[:, None] - key_blocks[None, :]) <= 1
    picked = jnp.any(chosen_rows[:, :, None] == key_blocks[None, None, :], axis=1)
    allowed = is_near | (key_blocks[None, :] == 0) | picked
    return jnp.repeat(jnp.repeat(allowed, blk_size, axis=0), blk_size, axis=1)


def gossip(update, distance, rep_count):
    if distance == 0:
        return update
    from_low = jax.tree.map(
        lambda part, own: part.astype(own.dtype),
        shifted(for_sending(update), "rep", distance),
        update,
    )
    from_high = jax.tree.map(
        lambda part, own: part.astype(own.dtype),
        shifted(for_sending(update), "rep", rep_count - distance),
        update,
    )
    return (update + from_low + from_high) / 3.0


def per_device(tokens, queries, ctx_grad, kv_weight, rand_blocks, step_count):
    tokens_here = tokens[0]
    query_here = queries[0]
    grad_here = ctx_grad[0]
    weight_here = kv_weight[0]
    seq_count = lax.axis_size(SEQ_AXES)
    rep_count = lax.axis_size("rep")
    seq_index = seq_position()
    tok_count = tokens_here.shape[0]
    kv_width = weight_here.shape[1]
    head_size = kv_width // 2
    blk_size = BLOCK
    blocks_dev = tok_count // blk_size
    inv_root = head_size ** (-0.5)
    kv_here = fold_rows(tokens_here, gather_seq(weight_here)).astype(jnp.bfloat16)
    kv_all = gather_other_first(kv_here)
    keys_all = kv_all[:, :head_size]
    values_all = kv_all[:, head_size:]
    half_n = seq_count // 2
    my_half = lax.axis_index("zh")
    order = jnp.concatenate([(1 - my_half) * half_n + jnp.arange(half_n), my_half * half_n + jnp.arange(half_n)])
    every_block = (order[:, None] * blocks_dev + jnp.arange(blocks_dev)[None, :]).reshape(-1).astype(jnp.int32)
    blocks_here = seq_index * blocks_dev + jnp.arange(blocks_dev, dtype=jnp.int32)
    chosen_here = lax.dynamic_slice_in_dim(rand_blocks, seq_index * blocks_dev, blocks_dev, 0)
    allowed = attend_mask(blocks_here, every_block, chosen_here, blk_size)
    scores = contract_cols(query_here, keys_all) * inv_root
    unnorm = jnp.where(allowed, jnp.exp(scores), jnp.float32(0.0))
    row_total = jnp.sum(unnorm, axis=1, keepdims=True)
    prob_rows = unnorm / row_total
    prob_low = prob_rows.astype(jnp.bfloat16)
    context = jnp.dot(prob_low, values_all, preferred_element_type=jnp.float32)
    row_delta = jnp.sum(grad_here.astype(jnp.float32) * context, axis=1, keepdims=True)
    prob_grad = contract_cols(grad_here, values_all)
    score_grad = (prob_rows * (prob_grad - row_delta) * inv_root).astype(jnp.bfloat16)
    query_grad = jnp.dot(score_grad, keys_all, preferred_element_type=jnp.float32).astype(
        jnp.bfloat16
    )
    key_terms = contract_rows(score_grad, query_here)
    value_terms = contract_rows(prob_low, grad_here)
    grad_terms = jnp.concatenate([key_terms, value_terms], axis=1).astype(jnp.bfloat16)
    half_rows = grad_terms.shape[0] // 2
    kv_grad = scatter_halves(grad_terms[:half_rows], grad_terms[half_rows:]).astype(jnp.bfloat16)
    tok_view = tokens_here.reshape(tok_count, 2, -1)
    tok_other = lax.dynamic_index_in_dim(tok_view, 1 - my_half, 1, keepdims=False)
    tok_mine = lax.dynamic_index_in_dim(tok_view, my_half, 1, keepdims=False)
    grad_slice = scatter_halves(
        contract_rows(tok_other, kv_grad).astype(jnp.bfloat16),
        contract_rows(tok_mine, kv_grad).astype(jnp.bfloat16),
    )
    branches = [
        partial(gossip, distance=(1 << level_idx) % rep_count, rep_count=rep_count)
        for level_idx in range(4)
    ]
    mixed_update = lax.switch(step_count[0] % 4, branches, grad_slice)
    return (mixed_update[None], query_grad[None])


def solution(mesh):
    rep_n, seq_n = mesh.devices.shape
    sub_mesh = Mesh(mesh.devices.reshape(rep_n, 2, seq_n // 4, 2), ("rep",) + SEQ_AXES)
    return jax.shard_map(
        per_device,
        mesh=sub_mesh,
        in_specs=(
            P("rep", SEQ_AXES, None),
            P("rep", SEQ_AXES, None),
            P("rep", SEQ_AXES, None),
            P("rep", SEQ_AXES, None),
            P(),
            P(),
        ),
        out_specs=(P("rep", SEQ_AXES, None), P("rep", SEQ_AXES, None)),
        check_vma=False,
    )
```

```python
from functools import partial

import jax
import jax.numpy as jnp
from jax import lax
from jax.sharding import Mesh
from jax.sharding import PartitionSpec as P


BLOCK = 64
SEQ_AXES = ("zh", "y", "c")


def for_sending(value):

    def short(part):
        return part.astype(jnp.bfloat16) if part.dtype == jnp.float32 else part

    return jax.tree.map(short, value)


def shifted(value, axis, steps):
    count = lax.axis_size(axis)
    pairs = [(source, (source + steps) % count) for source in range(count)]
    return lax.ppermute(value, axis, pairs)


def seq_position():
    return (lax.axis_index("zh") * lax.axis_size("y") + lax.axis_index("y")) * lax.axis_size(
        "c"
    ) + lax.axis_index("c")


def swap_zh(value):
    return lax.ppermute(value, "zh", [(0, 1), (1, 0)])


def spread_half(piece):
    count = lax.axis_size("y") * lax.axis_size("c")
    copies = jnp.broadcast_to(piece[None], (count,) + piece.shape)
    return lax.all_to_all(copies, ("y", "c"), 0, 0, tiled=False)


def gather_other_first(piece):
    from_other = swap_zh(piece)
    own_half = spread_half(piece)
    other_half = spread_half(from_other)
    return jnp.concatenate([other_half, own_half]).reshape((-1,) + piece.shape[1:])


def reduce_half(part):
    first_core = lax.axis_index("c") == 0
    keep = jnp.where(first_core, part[:, 0], part[:, 1])
    send = jnp.where(first_core, part[:, 1], part[:, 0])
    got = lax.ppermute(send, "c", [(0, 1), (1, 0)])
    summed = (keep.astype(jnp.float32) + got.astype(jnp.float32)).astype(jnp.bfloat16)
    spread = lax.all_to_all(summed, "y", 0, 0, tiled=False)
    return jnp.sum(spread.astype(jnp.float32), axis=0)


def scatter_halves(for_other, for_me):
    y_n, c_n = lax.axis_size("y"), lax.axis_size("c")
    shape = (y_n, c_n, for_other.shape[0] // (y_n * c_n)) + for_other.shape[1:]
    reduced = reduce_half(for_other.reshape(shape)).astype(jnp.bfloat16)
    got = swap_zh(reduced)
    kept = reduce_half(for_me.reshape(shape))
    return kept + got.astype(jnp.float32)


def fold_rows(tok_rows, row_piece):
    return jnp.dot(tok_rows, row_piece, preferred_element_type=jnp.float32)


def contract_rows(matrix_a, matrix_b):
    return lax.dot_general(
        matrix_a, matrix_b, (((0,), (0,)), ((), ())), preferred_element_type=jnp.float32
    )


def contract_cols(matrix_a, matrix_b):
    return lax.dot_general(
        matrix_a, matrix_b, (((1,), (1,)), ((), ())), preferred_element_type=jnp.float32
    )


def attend_mask(query_blocks, key_blocks, chosen_rows, blk_size):
    is_near = jnp.abs(query_blocks[:, None] - key_blocks[None, :]) <= 1
    picked = jnp.any(chosen_rows[:, :, None] == key_blocks[None, None, :], axis=1)
    allowed = is_near | (key_blocks[None, :] == 0) | picked
    return jnp.repeat(jnp.repeat(allowed, blk_size, axis=0), blk_size, axis=1)


def gossip(update, distance, rep_count):
    if distance == 0:
        return update
    from_low = jax.tree.map(
        lambda part, own: part.astype(own.dtype),
        shifted(for_sending(update), "rep", distance),
        update,
    )
    from_high = jax.tree.map(
        lambda part, own: part.astype(own.dtype),
        shifted(for_sending(update), "rep", rep_count - distance),
        update,
    )
    return (update + from_low + from_high) / 3.0


def per_device(tokens, queries, ctx_grad, kv_weight, rand_blocks, step_count):
    tokens_here = tokens[0]
    query_here = queries[0]
    grad_here = ctx_grad[0]
    weight_here = kv_weight[0]
    seq_count = lax.axis_size(SEQ_AXES)
    rep_count = lax.axis_size("rep")
    seq_index = seq_position()
    tok_count = tokens_here.shape[0]
    kv_width = weight_here.shape[1]
    head_size = kv_width // 2
    blk_size = BLOCK
    blocks_dev = tok_count // blk_size
    inv_root = head_size ** (-0.5)
    my_half = lax.axis_index("zh")
    tok_view = tokens_here.reshape(tok_count, 2, -1)
    tok_other = lax.dynamic_index_in_dim(tok_view, 1 - my_half, 1, keepdims=False)
    tok_mine = lax.dynamic_index_in_dim(tok_view, my_half, 1, keepdims=False)
    weight_rows = gather_other_first(weight_here)
    half_d = weight_rows.shape[0] // 2
    kv_here = (
        fold_rows(tok_other, weight_rows[:half_d]) + fold_rows(tok_mine, weight_rows[half_d:])
    ).astype(jnp.bfloat16)
    kv_all = gather_other_first(kv_here)
    keys_all = kv_all[:, :head_size]
    values_all = kv_all[:, head_size:]
    half_n = seq_count // 2
    order = jnp.concatenate([(1 - my_half) * half_n + jnp.arange(half_n), my_half * half_n + jnp.arange(half_n)])
    every_block = (order[:, None] * blocks_dev + jnp.arange(blocks_dev)[None, :]).reshape(-1).astype(jnp.int32)
    blocks_here = seq_index * blocks_dev + jnp.arange(blocks_dev, dtype=jnp.int32)
    chosen_here = lax.dynamic_slice_in_dim(rand_blocks, seq_index * blocks_dev, blocks_dev, 0)
    allowed = attend_mask(blocks_here, every_block, chosen_here, blk_size)
    scores = contract_cols(query_here, keys_all) * inv_root
    unnorm = jnp.where(allowed, jnp.exp(scores), jnp.float32(0.0))
    row_total = jnp.sum(unnorm, axis=1, keepdims=True)
    prob_rows = unnorm / row_total
    prob_low = prob_rows.astype(jnp.bfloat16)
    context = jnp.dot(prob_low, values_all, preferred_element_type=jnp.float32)
    row_delta = jnp.sum(grad_here.astype(jnp.float32) * context, axis=1, keepdims=True)
    prob_grad = contract_cols(grad_here, values_all)
    score_grad = (prob_rows * (prob_grad - row_delta) * inv_root).astype(jnp.bfloat16)
    query_grad = jnp.dot(score_grad, keys_all, preferred_element_type=jnp.float32).astype(
        jnp.bfloat16
    )
    key_terms = contract_rows(score_grad, query_here)
    value_terms = contract_rows(prob_low, grad_here)
    grad_terms = jnp.concatenate([key_terms, value_terms], axis=1).astype(jnp.bfloat16)
    half_rows = grad_terms.shape[0] // 2
    kv_grad = scatter_halves(grad_terms[:half_rows], grad_terms[half_rows:]).astype(jnp.bfloat16)
    grad_slice = scatter_halves(
        contract_rows(tok_other, kv_grad).astype(jnp.bfloat16),
        contract_rows(tok_mine, kv_grad).astype(jnp.bfloat16),
    )
    branches = [
        partial(gossip, distance=(1 << level_idx) % rep_count, rep_count=rep_count)
        for level_idx in range(4)
    ]
    mixed_update = lax.switch(step_count[0] % 4, branches, grad_slice)
    return (mixed_update[None], query_grad[None])


def solution(mesh):
    rep_n, seq_n = mesh.devices.shape
    sub_mesh = Mesh(mesh.devices.reshape(rep_n, 2, seq_n // 4, 2), ("rep",) + SEQ_AXES)
    return jax.shard_map(
        per_device,
        mesh=sub_mesh,
        in_specs=(
            P("rep", SEQ_AXES, None),
            P("rep", SEQ_AXES, None),
            P("rep", SEQ_AXES, None),
            P("rep", SEQ_AXES, None),
            P(),
            P(),
        ),
        out_specs=(P("rep", SEQ_AXES, None), P("rep", SEQ_AXES, None)),
        check_vma=False,
    )
```

```python
from functools import partial

import jax
import jax.numpy as jnp
from jax import lax
from jax.sharding import Mesh
from jax.sharding import PartitionSpec as P


BLOCK = 64
SEQ_AXES = ("zh", "y", "c")


def for_sending(value):

    def short(part):
        return part.astype(jnp.bfloat16) if part.dtype == jnp.float32 else part

    return jax.tree.map(short, value)


def shifted(value, axis, steps):
    count = lax.axis_size(axis)
    pairs = [(source, (source + steps) % count) for source in range(count)]
    return lax.ppermute(value, axis, pairs)


def seq_position():
    return (lax.axis_index("zh") * lax.axis_size("y") + lax.axis_index("y")) * lax.axis_size(
        "c"
    ) + lax.axis_index("c")


def swap_zh(value):
    return lax.ppermute(value, "zh", [(0, 1), (1, 0)])


def spread_half(piece):
    count = lax.axis_size("y") * lax.axis_size("c")
    copies = jnp.broadcast_to(piece[None], (count,) + piece.shape)
    return lax.all_to_all(copies, ("y", "c"), 0, 0, tiled=False)


def gather_seq(piece):
    from_other = swap_zh(piece)
    own_half = spread_half(piece)
    other_half = spread_half(from_other)
    first_own = lax.axis_index("zh") == 0
    low = jnp.where(first_own, own_half, other_half)
    high = jnp.where(first_own, other_half, own_half)
    return jnp.concatenate([low, high]).reshape((-1,) + piece.shape[1:])


def gather_other_first(piece):
    from_other = swap_zh(piece)
    own_half = spread_half(piece)
    other_half = spread_half(from_other)
    return jnp.concatenate([other_half, own_half]).reshape((-1,) + piece.shape[1:])


def reduce_half(part):
    first_core = lax.axis_index("c") == 0
    keep = jnp.where(first_core, part[:, 0], part[:, 1])
    send = jnp.where(first_core, part[:, 1], part[:, 0])
    got = lax.ppermute(send, "c", [(0, 1), (1, 0)])
    summed = (keep.astype(jnp.float32) + got.astype(jnp.float32)).astype(jnp.bfloat16)
    spread = lax.all_to_all(summed, "y", 0, 0, tiled=False)
    return jnp.sum(spread.astype(jnp.float32), axis=0)


def scatter_halves(for_other, for_me):
    y_n, c_n = lax.axis_size("y"), lax.axis_size("c")
    shape = (y_n, c_n, for_other.shape[0] // (y_n * c_n)) + for_other.shape[1:]
    reduced = reduce_half(for_other.reshape(shape)).astype(jnp.bfloat16)
    got = swap_zh(reduced)
    kept = reduce_half(for_me.reshape(shape))
    return kept + got.astype(jnp.float32)


def fold_rows(tok_rows, row_piece):
    return jnp.dot(tok_rows, row_piece, preferred_element_type=jnp.float32)


def contract_rows(matrix_a, matrix_b):
    return lax.dot_general(
        matrix_a, matrix_b, (((0,), (0,)), ((), ())), preferred_element_type=jnp.float32
    )


def contract_cols(matrix_a, matrix_b):
    return lax.dot_general(
        matrix_a, matrix_b, (((1,), (1,)), ((), ())), preferred_element_type=jnp.float32
    )


def attend_mask(query_blocks, key_blocks, chosen_rows, blk_size):
    is_near = jnp.abs(query_blocks[:, None] - key_blocks[None, :]) <= 1
    picked = jnp.any(chosen_rows[:, :, None] == key_blocks[None, None, :], axis=1)
    allowed = is_near | (key_blocks[None, :] == 0) | picked
    return jnp.repeat(jnp.repeat(allowed, blk_size, axis=0), blk_size, axis=1)


def gossip(update, distance, rep_count):
    if distance == 0:
        return update
    from_low = jax.tree.map(
        lambda part, own: part.astype(own.dtype),
        shifted(for_sending(update), "rep", distance),
        update,
    )
    from_high = jax.tree.map(
        lambda part, own: part.astype(own.dtype),
        shifted(for_sending(update), "rep", rep_count - distance),
        update,
    )
    return (update + from_low + from_high) / 3.0


def per_device(tokens, queries, ctx_grad, kv_weight, rand_blocks, step_count):
    tokens_here = tokens[0]
    query_here = queries[0]
    grad_here = ctx_grad[0]
    weight_here = kv_weight[0]
    seq_count = lax.axis_size(SEQ_AXES)
    rep_count = lax.axis_size("rep")
    seq_index = seq_position()
    tok_count = tokens_here.shape[0]
    kv_width = weight_here.shape[1]
    head_size = kv_width // 2
    blk_size = BLOCK
    blocks_dev = tok_count // blk_size
    inv_root = head_size ** (-0.5)
    kv_here = fold_rows(tokens_here, gather_seq(weight_here)).astype(jnp.bfloat16)
    kv_all = gather_other_first(kv_here)
    keys_all = kv_all[:, :head_size]
    values_all = kv_all[:, head_size:]
    half_n = seq_count // 2
    my_half = lax.axis_index("zh")
    order = jnp.concatenate([(1 - my_half) * half_n + jnp.arange(half_n), my_half * half_n + jnp.arange(half_n)])
    every_block = (order[:, None] * blocks_dev + jnp.arange(blocks_dev)[None, :]).reshape(-1).astype(jnp.int32)
    blocks_here = seq_index * blocks_dev + jnp.arange(blocks_dev, dtype=jnp.int32)
    chosen_here = lax.dynamic_slice_in_dim(rand_blocks, seq_index * blocks_dev, blocks_dev, 0)
    allowed = attend_mask(blocks_here, every_block, chosen_here, blk_size)
    scores = contract_cols(query_here, keys_all) * inv_root
    unnorm = jnp.where(allowed, jnp.exp(scores), jnp.float32(0.0))
    row_total = jnp.sum(unnorm, axis=1, keepdims=True)
    prob_rows = unnorm / row_total
    prob_low = prob_rows.astype(jnp.bfloat16)
    context = jnp.dot(prob_low, values_all, preferred_element_type=jnp.float32)
    row_delta = jnp.sum(grad_here.astype(jnp.float32) * context, axis=1, keepdims=True)
    prob_grad = contract_cols(grad_here, values_all)
    score_grad = (prob_rows * (prob_grad - row_delta) * inv_root).astype(jnp.bfloat16)
    query_grad = jnp.dot(score_grad, keys_all, preferred_element_type=jnp.float32).astype(
        jnp.bfloat16
    )
    half_keys = score_grad.shape[1] // 2

    def terms_for(cols):
        return jnp.concatenate(
            [contract_rows(score_grad[:, cols], query_here), contract_rows(prob_low[:, cols], grad_here)],
            axis=1,
        ).astype(jnp.bfloat16)

    kv_grad = scatter_halves(
        terms_for(slice(0, half_keys)), terms_for(slice(half_keys, None))
    ).astype(jnp.bfloat16)
    tok_view = tokens_here.reshape(tok_count, 2, -1)
    tok_other = lax.dynamic_index_in_dim(tok_view, 1 - my_half, 1, keepdims=False)
    tok_mine = lax.dynamic_index_in_dim(tok_view, my_half, 1, keepdims=False)
    grad_slice = scatter_halves(
        contract_rows(tok_other, kv_grad).astype(jnp.bfloat16),
        contract_rows(tok_mine, kv_grad).astype(jnp.bfloat16),
    )
    branches = [
        partial(gossip, distance=(1 << level_idx) % rep_count, rep_count=rep_count)
        for level_idx in range(4)
    ]
    mixed_update = lax.switch(step_count[0] % 4, branches, grad_slice)
    return (mixed_update[None], query_grad[None])


def solution(mesh):
    rep_n, seq_n = mesh.devices.shape
    sub_mesh = Mesh(mesh.devices.reshape(rep_n, 2, seq_n // 4, 2), ("rep",) + SEQ_AXES)
    return jax.shard_map(
        per_device,
        mesh=sub_mesh,
        in_specs=(
            P("rep", SEQ_AXES, None),
            P("rep", SEQ_AXES, None),
            P("rep", SEQ_AXES, None),
            P("rep", SEQ_AXES, None),
            P(),
            P(),
        ),
        out_specs=(P("rep", SEQ_AXES, None), P("rep", SEQ_AXES, None)),
        check_vma=False,
    )
```

```python
from functools import partial

import jax
import jax.numpy as jnp
from jax import lax
from jax.sharding import Mesh
from jax.sharding import PartitionSpec as P


BLOCK = 64
SEQ_AXES = ("zh", "y", "c")


def for_sending(value):

    def short(part):
        return part.astype(jnp.bfloat16) if part.dtype == jnp.float32 else part

    return jax.tree.map(short, value)


def shifted(value, axis, steps):
    count = lax.axis_size(axis)
    pairs = [(source, (source + steps) % count) for source in range(count)]
    return lax.ppermute(value, axis, pairs)


def seq_position():
    return (lax.axis_index("zh") * lax.axis_size("y") + lax.axis_index("y")) * lax.axis_size(
        "c"
    ) + lax.axis_index("c")


def swap_zh(value):
    return lax.ppermute(value, "zh", [(0, 1), (1, 0)])


def spread_half(piece):
    count = lax.axis_size("y") * lax.axis_size("c")
    copies = jnp.broadcast_to(piece[None], (count,) + piece.shape)
    return lax.all_to_all(copies, ("y", "c"), 0, 0, tiled=False)


def gather_seq(piece):
    from_other = swap_zh(piece)
    own_half = spread_half(piece)
    other_half = spread_half(from_other)
    first_own = lax.axis_index("zh") == 0
    low = jnp.where(first_own, own_half, other_half)
    high = jnp.where(first_own, other_half, own_half)
    return jnp.concatenate([low, high]).reshape((-1,) + piece.shape[1:])


def gather_other_first(piece):
    from_other = swap_zh(piece)
    own_half = spread_half(piece)
    other_half = spread_half(from_other)
    return jnp.concatenate([other_half, own_half]).reshape((-1,) + piece.shape[1:])


def reduce_half(part):
    first_core = lax.axis_index("c") == 0
    keep = jnp.where(first_core, part[:, 0], part[:, 1])
    send = jnp.where(first_core, part[:, 1], part[:, 0])
    got = lax.ppermute(send, "c", [(0, 1), (1, 0)])
    summed = (keep.astype(jnp.float32) + got.astype(jnp.float32)).astype(jnp.bfloat16)
    spread = lax.all_to_all(summed, "y", 0, 0, tiled=False)
    return jnp.sum(spread.astype(jnp.float32), axis=0)


def scatter_halves(for_other, for_me):
    y_n, c_n = lax.axis_size("y"), lax.axis_size("c")
    shape = (y_n, c_n, for_other.shape[0] // (y_n * c_n)) + for_other.shape[1:]
    reduced = reduce_half(for_other.reshape(shape)).astype(jnp.bfloat16)
    got = swap_zh(reduced)
    kept = reduce_half(for_me.reshape(shape))
    return kept + got.astype(jnp.float32)


def fold_rows(tok_rows, row_piece):
    return jnp.dot(tok_rows, row_piece, preferred_element_type=jnp.float32)


def contract_rows(matrix_a, matrix_b):
    return lax.dot_general(
        matrix_a, matrix_b, (((0,), (0,)), ((), ())), preferred_element_type=jnp.float32
    )


def contract_cols(matrix_a, matrix_b):
    return lax.dot_general(
        matrix_a, matrix_b, (((1,), (1,)), ((), ())), preferred_element_type=jnp.float32
    )


def attend_mask(query_blocks, key_blocks, chosen_rows, blk_size):
    is_near = jnp.abs(query_blocks[:, None] - key_blocks[None, :]) <= 1
    picked = jnp.any(chosen_rows[:, :, None] == key_blocks[None, None, :], axis=1)
    allowed = is_near | (key_blocks[None, :] == 0) | picked
    return jnp.repeat(jnp.repeat(allowed, blk_size, axis=0), blk_size, axis=1)


def gossip(pair, distance, rep_count):
    update, sent = pair
    if distance == 0:
        return update
    from_low = shifted(sent, "rep", distance).astype(update.dtype)
    from_high = shifted(sent, "rep", rep_count - distance).astype(update.dtype)
    return (update + from_low + from_high) / 3.0


def per_device(tokens, queries, ctx_grad, kv_weight, rand_blocks, step_count):
    tokens_here = tokens[0]
    query_here = queries[0]
    grad_here = ctx_grad[0]
    weight_here = kv_weight[0]
    seq_count = lax.axis_size(SEQ_AXES)
    rep_count = lax.axis_size("rep")
    seq_index = seq_position()
    tok_count = tokens_here.shape[0]
    kv_width = weight_here.shape[1]
    head_size = kv_width // 2
    blk_size = BLOCK
    blocks_dev = tok_count // blk_size
    inv_root = head_size ** (-0.5)
    kv_here = fold_rows(tokens_here, gather_seq(weight_here)).astype(jnp.bfloat16)
    kv_all = gather_other_first(kv_here)
    keys_all = kv_all[:, :head_size]
    values_all = kv_all[:, head_size:]
    half_n = seq_count // 2
    my_half = lax.axis_index("zh")
    order = jnp.concatenate([(1 - my_half) * half_n + jnp.arange(half_n), my_half * half_n + jnp.arange(half_n)])
    every_block = (order[:, None] * blocks_dev + jnp.arange(blocks_dev)[None, :]).reshape(-1).astype(jnp.int32)
    blocks_here = seq_index * blocks_dev + jnp.arange(blocks_dev, dtype=jnp.int32)
    chosen_here = lax.dynamic_slice_in_dim(rand_blocks, seq_index * blocks_dev, blocks_dev, 0)
    allowed = attend_mask(blocks_here, every_block, chosen_here, blk_size)
    scores = contract_cols(query_here, keys_all) * inv_root
    unnorm = jnp.where(allowed, jnp.exp(scores), jnp.float32(0.0))
    row_total = jnp.sum(unnorm, axis=1, keepdims=True)
    prob_rows = unnorm / row_total
    prob_low = prob_rows.astype(jnp.bfloat16)
    context = jnp.dot(prob_low, values_all, preferred_element_type=jnp.float32)
    row_delta = jnp.sum(grad_here.astype(jnp.float32) * context, axis=1, keepdims=True)
    prob_grad = contract_cols(grad_here, values_all)
    score_grad = (prob_rows * (prob_grad - row_delta) * inv_root).astype(jnp.bfloat16)
    query_grad = jnp.dot(score_grad, keys_all, preferred_element_type=jnp.float32).astype(
        jnp.bfloat16
    )
    half_keys = score_grad.shape[1] // 2

    def terms_for(cols):
        return jnp.concatenate(
            [contract_rows(score_grad[:, cols], query_here), contract_rows(prob_low[:, cols], grad_here)],
            axis=1,
        ).astype(jnp.bfloat16)

    kv_grad = scatter_halves(
        terms_for(slice(0, half_keys)), terms_for(slice(half_keys, None))
    ).astype(jnp.bfloat16)
    tok_view = tokens_here.reshape(tok_count, 2, -1)
    tok_other = lax.dynamic_index_in_dim(tok_view, 1 - my_half, 1, keepdims=False)
    tok_mine = lax.dynamic_index_in_dim(tok_view, my_half, 1, keepdims=False)
    grad_slice = scatter_halves(
        contract_rows(tok_other, kv_grad).astype(jnp.bfloat16),
        contract_rows(tok_mine, kv_grad).astype(jnp.bfloat16),
    )
    branches = [
        partial(gossip, distance=(1 << level_idx) % rep_count, rep_count=rep_count)
        for level_idx in range(4)
    ]
    mixed_update = lax.switch(step_count[0] % 4, branches, (grad_slice, for_sending(grad_slice)))
    return (mixed_update[None], query_grad[None])


def solution(mesh):
    rep_n, seq_n = mesh.devices.shape
    sub_mesh = Mesh(mesh.devices.reshape(rep_n, 2, seq_n // 4, 2), ("rep",) + SEQ_AXES)
    return jax.shard_map(
        per_device,
        mesh=sub_mesh,
        in_specs=(
            P("rep", SEQ_AXES, None),
            P("rep", SEQ_AXES, None),
            P("rep", SEQ_AXES, None),
            P("rep", SEQ_AXES, None),
            P(),
            P(),
        ),
        out_specs=(P("rep", SEQ_AXES, None), P("rep", SEQ_AXES, None)),
        check_vma=False,
    )
```

```python
from functools import partial

import jax
import jax.numpy as jnp
from jax import lax
from jax.sharding import Mesh
from jax.sharding import PartitionSpec as P


BLOCK = 64
SEQ_AXES = ("zh", "y", "c")


def for_sending(value):

    def short(part):
        return part.astype(jnp.bfloat16) if part.dtype == jnp.float32 else part

    return jax.tree.map(short, value)


def shifted(value, axis, steps):
    count = lax.axis_size(axis)
    pairs = [(source, (source + steps) % count) for source in range(count)]
    return lax.ppermute(value, axis, pairs)


def seq_position():
    return (lax.axis_index("zh") * lax.axis_size("y") + lax.axis_index("y")) * lax.axis_size(
        "c"
    ) + lax.axis_index("c")


def swap_zh(value):
    return lax.ppermute(value, "zh", [(0, 1), (1, 0)])


def spread_half(piece):
    count = lax.axis_size("y") * lax.axis_size("c")
    copies = jnp.broadcast_to(piece[None], (count,) + piece.shape)
    return lax.all_to_all(copies, ("y", "c"), 0, 0, tiled=False)


def gather_seq(piece):
    from_other = swap_zh(piece)
    own_half = spread_half(piece)
    other_half = spread_half(from_other)
    first_own = lax.axis_index("zh") == 0
    low = jnp.where(first_own, own_half, other_half)
    high = jnp.where(first_own, other_half, own_half)
    return jnp.concatenate([low, high]).reshape((-1,) + piece.shape[1:])


def gather_other_first(piece):
    from_other = swap_zh(piece)
    own_half = spread_half(piece)
    other_half = spread_half(from_other)
    return jnp.concatenate([other_half, own_half]).reshape((-1,) + piece.shape[1:])


def reduce_half(part):
    first_core = lax.axis_index("c") == 0
    keep = jnp.where(first_core, part[:, 0], part[:, 1])
    send = jnp.where(first_core, part[:, 1], part[:, 0])
    got = lax.ppermute(send, "c", [(0, 1), (1, 0)])
    summed = (keep.astype(jnp.float32) + got.astype(jnp.float32)).astype(jnp.bfloat16)
    spread = lax.all_to_all(summed, "y", 0, 0, tiled=False)
    return jnp.sum(spread.astype(jnp.float32), axis=0)


def scatter_halves(for_other, for_me):
    y_n, c_n = lax.axis_size("y"), lax.axis_size("c")
    shape = (y_n, c_n, for_other.shape[0] // (y_n * c_n)) + for_other.shape[1:]
    reduced = reduce_half(for_other.reshape(shape)).astype(jnp.bfloat16)
    got = swap_zh(reduced)
    kept = reduce_half(for_me.reshape(shape))
    return kept + got.astype(jnp.float32)


def fold_rows(tok_rows, row_piece):
    return jnp.dot(tok_rows, row_piece, preferred_element_type=jnp.float32)


def contract_rows(matrix_a, matrix_b):
    return lax.dot_general(
        matrix_a, matrix_b, (((0,), (0,)), ((), ())), preferred_element_type=jnp.float32
    )


def contract_cols(matrix_a, matrix_b):
    return lax.dot_general(
        matrix_a, matrix_b, (((1,), (1,)), ((), ())), preferred_element_type=jnp.float32
    )


def attend_mask(query_blocks, key_blocks, chosen_rows, blk_size):
    is_near = jnp.abs(query_blocks[:, None] - key_blocks[None, :]) <= 1
    picked = jnp.any(chosen_rows[:, :, None] == key_blocks[None, None, :], axis=1)
    allowed = is_near | (key_blocks[None, :] == 0) | picked
    return jnp.repeat(jnp.repeat(allowed, blk_size, axis=0), blk_size, axis=1)


def gossip(update, distance, rep_count):
    if distance == 0:
        return update
    from_low = jax.tree.map(
        lambda part, own: part.astype(own.dtype),
        shifted(for_sending(update), "rep", distance),
        update,
    )
    from_high = jax.tree.map(
        lambda part, own: part.astype(own.dtype),
        shifted(for_sending(update), "rep", rep_count - distance),
        update,
    )
    return (update + from_low + from_high) / 3.0


def per_device(tokens, queries, ctx_grad, kv_weight, rand_blocks, step_count):
    tokens_here = tokens[0]
    query_here = queries[0]
    grad_here = ctx_grad[0]
    weight_here = kv_weight[0]
    seq_count = lax.axis_size(SEQ_AXES)
    rep_count = lax.axis_size("rep")
    seq_index = seq_position()
    tok_count = tokens_here.shape[0]
    kv_width = weight_here.shape[1]
    head_size = kv_width // 2
    blk_size = BLOCK
    blocks_dev = tok_count // blk_size
    inv_root = head_size ** (-0.5)
    kv_here = fold_rows(tokens_here, gather_seq(weight_here)).astype(jnp.bfloat16)
    kv_all = gather_other_first(kv_here)
    keys_all = kv_all[:, :head_size]
    values_all = kv_all[:, head_size:]
    half_n = seq_count // 2
    my_half = lax.axis_index("zh")
    order = jnp.concatenate([(1 - my_half) * half_n + jnp.arange(half_n), my_half * half_n + jnp.arange(half_n)])
    every_block = (order[:, None] * blocks_dev + jnp.arange(blocks_dev)[None, :]).reshape(-1).astype(jnp.int32)
    blocks_here = seq_index * blocks_dev + jnp.arange(blocks_dev, dtype=jnp.int32)
    chosen_here = lax.dynamic_slice_in_dim(rand_blocks, seq_index * blocks_dev, blocks_dev, 0)
    allowed = attend_mask(blocks_here, every_block, chosen_here, blk_size)
    scores = contract_cols(query_here, keys_all) * inv_root
    unnorm = jnp.where(allowed, jnp.exp(scores), jnp.float32(0.0))
    row_total = jnp.sum(unnorm, axis=1, keepdims=True)
    prob_rows = unnorm / row_total
    prob_low = prob_rows.astype(jnp.bfloat16)
    context = jnp.dot(prob_low, values_all, preferred_element_type=jnp.float32)
    row_delta = jnp.sum(grad_here.astype(jnp.float32) * context, axis=1, keepdims=True)
    prob_grad = contract_cols(grad_here, values_all)
    score_grad = (prob_rows * (prob_grad - row_delta) * inv_root).astype(jnp.bfloat16)
    query_grad = jnp.dot(score_grad, keys_all, preferred_element_type=jnp.float32).astype(
        jnp.bfloat16
    )
    half_keys = score_grad.shape[1] // 2

    def terms_for(cols):
        return jnp.concatenate(
            [contract_rows(score_grad[:, cols], query_here), contract_rows(prob_low[:, cols], grad_here)],
            axis=1,
        ).astype(jnp.bfloat16)

    kv_grad = scatter_halves(
        terms_for(slice(0, half_keys)), terms_for(slice(half_keys, None))
    ).astype(jnp.bfloat16)
    weight_terms = contract_rows(tokens_here, kv_grad).astype(jnp.bfloat16)
    half_d = weight_terms.shape[0] // 2
    low_rows, high_rows = weight_terms[:half_d], weight_terms[half_d:]
    first_own = my_half == 0
    grad_slice = scatter_halves(
        jnp.where(first_own, high_rows, low_rows), jnp.where(first_own, low_rows, high_rows)
    )
    branches = [
        partial(gossip, distance=(1 << level_idx) % rep_count, rep_count=rep_count)
        for level_idx in range(4)
    ]
    mixed_update = lax.switch(step_count[0] % 4, branches, grad_slice)
    return (mixed_update[None], query_grad[None])


def solution(mesh):
    rep_n, seq_n = mesh.devices.shape
    sub_mesh = Mesh(mesh.devices.reshape(rep_n, 2, seq_n // 4, 2), ("rep",) + SEQ_AXES)
    return jax.shard_map(
        per_device,
        mesh=sub_mesh,
        in_specs=(
            P("rep", SEQ_AXES, None),
            P("rep", SEQ_AXES, None),
            P("rep", SEQ_AXES, None),
            P("rep", SEQ_AXES, None),
            P(),
            P(),
        ),
        out_specs=(P("rep", SEQ_AXES, None), P("rep", SEQ_AXES, None)),
        check_vma=False,
    )
```

```python
from functools import partial

import jax
import jax.numpy as jnp
from jax import lax
from jax.sharding import Mesh
from jax.sharding import PartitionSpec as P


BLOCK = 64
SEQ_AXES = ("zh", "y", "c")


def for_sending(value):

    def short(part):
        return part.astype(jnp.bfloat16) if part.dtype == jnp.float32 else part

    return jax.tree.map(short, value)


def shifted(value, axis, steps):
    count = lax.axis_size(axis)
    pairs = [(source, (source + steps) % count) for source in range(count)]
    return lax.ppermute(value, axis, pairs)


def seq_position():
    return (lax.axis_index("zh") * lax.axis_size("y") + lax.axis_index("y")) * lax.axis_size(
        "c"
    ) + lax.axis_index("c")


def swap_zh(value):
    return lax.ppermute(value, "zh", [(0, 1), (1, 0)])


def spread_half(piece):
    count = lax.axis_size("y") * lax.axis_size("c")
    copies = jnp.broadcast_to(piece[None], (count,) + piece.shape)
    return lax.all_to_all(copies, ("y", "c"), 0, 0, tiled=False)


def gather_seq(piece):
    from_other = swap_zh(piece)
    own_half = spread_half(piece)
    other_half = spread_half(from_other)
    first_own = lax.axis_index("zh") == 0
    low = jnp.where(first_own, own_half, other_half)
    high = jnp.where(first_own, other_half, own_half)
    return jnp.concatenate([low, high]).reshape((-1,) + piece.shape[1:])


def gather_other_first(piece):
    from_other = swap_zh(piece)
    own_half = spread_half(piece)
    other_half = spread_half(from_other)
    return jnp.concatenate([other_half, own_half]).reshape((-1,) + piece.shape[1:])


def reduce_half(part):
    first_core = lax.axis_index("c") == 0
    keep = jnp.where(first_core, part[:, 0], part[:, 1])
    send = jnp.where(first_core, part[:, 1], part[:, 0])
    got = lax.ppermute(send, "c", [(0, 1), (1, 0)])
    summed = (keep.astype(jnp.float32) + got.astype(jnp.float32)).astype(jnp.bfloat16)
    spread = lax.all_to_all(summed, "y", 0, 0, tiled=False)
    return jnp.sum(spread.astype(jnp.float32), axis=0)


def scatter_halves(for_other, for_me):
    y_n, c_n = lax.axis_size("y"), lax.axis_size("c")
    shape = (y_n, c_n, for_other.shape[0] // (y_n * c_n)) + for_other.shape[1:]
    reduced = reduce_half(for_other.reshape(shape)).astype(jnp.bfloat16)
    got = swap_zh(reduced)
    for_me = for_me() if callable(for_me) else for_me
    kept = reduce_half(for_me.reshape(shape))
    return kept + got.astype(jnp.float32)


def fold_rows(tok_rows, row_piece):
    return jnp.dot(tok_rows, row_piece, preferred_element_type=jnp.float32)


def contract_rows(matrix_a, matrix_b):
    return lax.dot_general(
        matrix_a, matrix_b, (((0,), (0,)), ((), ())), preferred_element_type=jnp.float32
    )


def contract_cols(matrix_a, matrix_b):
    return lax.dot_general(
        matrix_a, matrix_b, (((1,), (1,)), ((), ())), preferred_element_type=jnp.float32
    )


def attend_mask(query_blocks, key_blocks, chosen_rows, blk_size):
    is_near = jnp.abs(query_blocks[:, None] - key_blocks[None, :]) <= 1
    picked = jnp.any(chosen_rows[:, :, None] == key_blocks[None, None, :], axis=1)
    allowed = is_near | (key_blocks[None, :] == 0) | picked
    return jnp.repeat(jnp.repeat(allowed, blk_size, axis=0), blk_size, axis=1)


def gossip(update, distance, rep_count):
    if distance == 0:
        return update
    from_low = jax.tree.map(
        lambda part, own: part.astype(own.dtype),
        shifted(for_sending(update), "rep", distance),
        update,
    )
    from_high = jax.tree.map(
        lambda part, own: part.astype(own.dtype),
        shifted(for_sending(update), "rep", rep_count - distance),
        update,
    )
    return (update + from_low + from_high) / 3.0


def per_device(tokens, queries, ctx_grad, kv_weight, rand_blocks, step_count):
    tokens_here = tokens[0]
    query_here = queries[0]
    grad_here = ctx_grad[0]
    weight_here = kv_weight[0]
    seq_count = lax.axis_size(SEQ_AXES)
    rep_count = lax.axis_size("rep")
    seq_index = seq_position()
    tok_count = tokens_here.shape[0]
    kv_width = weight_here.shape[1]
    head_size = kv_width // 2
    blk_size = BLOCK
    blocks_dev = tok_count // blk_size
    inv_root = head_size ** (-0.5)
    kv_here = fold_rows(tokens_here, gather_seq(weight_here)).astype(jnp.bfloat16)
    kv_all = gather_other_first(kv_here)
    keys_all = kv_all[:, :head_size]
    values_all = kv_all[:, head_size:]
    half_n = seq_count // 2
    my_half = lax.axis_index("zh")
    order = jnp.concatenate([(1 - my_half) * half_n + jnp.arange(half_n), my_half * half_n + jnp.arange(half_n)])
    every_block = (order[:, None] * blocks_dev + jnp.arange(blocks_dev)[None, :]).reshape(-1).astype(jnp.int32)
    blocks_here = seq_index * blocks_dev + jnp.arange(blocks_dev, dtype=jnp.int32)
    chosen_here = lax.dynamic_slice_in_dim(rand_blocks, seq_index * blocks_dev, blocks_dev, 0)
    allowed = attend_mask(blocks_here, every_block, chosen_here, blk_size)
    scores = contract_cols(query_here, keys_all) * inv_root
    unnorm = jnp.where(allowed, jnp.exp(scores), jnp.float32(0.0))
    row_total = jnp.sum(unnorm, axis=1, keepdims=True)
    prob_rows = unnorm / row_total
    prob_low = prob_rows.astype(jnp.bfloat16)
    context = jnp.dot(prob_low, values_all, preferred_element_type=jnp.float32)
    row_delta = jnp.sum(grad_here.astype(jnp.float32) * context, axis=1, keepdims=True)
    prob_grad = contract_cols(grad_here, values_all)
    score_grad = (prob_rows * (prob_grad - row_delta) * inv_root).astype(jnp.bfloat16)
    query_grad = jnp.dot(score_grad, keys_all, preferred_element_type=jnp.float32).astype(
        jnp.bfloat16
    )
    half_keys = score_grad.shape[1] // 2

    def terms_for(cols):
        return jnp.concatenate(
            [contract_rows(score_grad[:, cols], query_here), contract_rows(prob_low[:, cols], grad_here)],
            axis=1,
        ).astype(jnp.bfloat16)

    kv_grad = scatter_halves(
        terms_for(slice(0, half_keys)), lambda: terms_for(slice(half_keys, None))
    ).astype(jnp.bfloat16)
    tok_view = tokens_here.reshape(tok_count, 2, -1)
    tok_other = lax.dynamic_index_in_dim(tok_view, 1 - my_half, 1, keepdims=False)
    tok_mine = lax.dynamic_index_in_dim(tok_view, my_half, 1, keepdims=False)
    grad_slice = scatter_halves(
        contract_rows(tok_other, kv_grad).astype(jnp.bfloat16), contract_rows(tok_mine, kv_grad).astype(jnp.bfloat16)
    )
    branches = [
        partial(gossip, distance=(1 << level_idx) % rep_count, rep_count=rep_count)
        for level_idx in range(4)
    ]
    mixed_update = lax.switch(step_count[0] % 4, branches, grad_slice)
    return (mixed_update[None], query_grad[None])


def solution(mesh):
    rep_n, seq_n = mesh.devices.shape
    sub_mesh = Mesh(mesh.devices.reshape(rep_n, 2, seq_n // 4, 2), ("rep",) + SEQ_AXES)
    return jax.shard_map(
        per_device,
        mesh=sub_mesh,
        in_specs=(
            P("rep", SEQ_AXES, None),
            P("rep", SEQ_AXES, None),
            P("rep", SEQ_AXES, None),
            P("rep", SEQ_AXES, None),
            P(),
            P(),
        ),
        out_specs=(P("rep", SEQ_AXES, None), P("rep", SEQ_AXES, None)),
        check_vma=False,
    )
```
